512 devices in a mesh: dp: 64 (over y, x, core), mp: 8 (over z).
Axes of the slice: x: 4, y: 8, z: 8, core: 2. Of those that a mesh axis runs over, the one named last changes fastest.
Arguments:
- x_in: bfloat16 [2, 1024, 4096], P(None, 'dp')
- queries: bfloat16 [2, 1024, 32, 128], P(None, ('dp', 'mp'))
- new_keys: bfloat16 [2, 1024, 2, 128], P(None, ('dp', 'mp'))
- new_values: bfloat16 [2, 1024, 2, 128], P(None, ('dp', 'mp')), may hold values from -6 to 6
- cache_keys: bfloat16 [1024, 512, 2, 128], P(('dp', 'mp'))
- cache_values: bfloat16 [1024, 512, 2, 128], P(('dp', 'mp')), may hold values from -6 to 6
- lengths: int32 [1024], P(('dp', 'mp')), may hold values from 64 to 512, as said below
- o_weight: bfloat16 [4096, 4096], P('mp', 'dp'), may hold values from -0.375 to 0.375
- norm_gain: float32 [4096], replicated, may hold values from 0.1 to 1.9
- router: bfloat16 [4096, 64], replicated
- routes: int32 [2, 1024, 8], P(None, 'dp'), may hold values from 0 to 63, all different within a row; in each aligned block of 16 rows (0 to 15, 16 to 31, ..., all dimensions but the last counted through in order) at most 3 rows name the same one
- expert_shards: bfloat16 [3, 64, 4096, 1024], P(None, None, ('dp', 'mp')), may hold values from -0.1875 to 0.1875
Outputs:
- mixed_out: bfloat16 [2, 1024, 4096], P(None, 'dp', 'mp')
The draws below stay inside these ranges and needn't reach their ends.
Inputs may be any that keep to these rules, and one draw needn't show every extreme that they name: `routes`: within each aligned block of the 16 rows of one index of dp at one step, no expert is named by more than 3 rows; in some block one expert is named by exactly 3 rows. `lengths`: among the 2 rows of each device one has length 512.
All inputs are finite; a program needn't handle non-finite values.
Results may differ from the reference program's by a relative error of at most 0.019.
The reference program's roundings to bfloat16 on the way count: a program that leaves them out, or rounds other values in their place, can miss the bound.
Values may be sent and summed in bfloat16 or wider, within the bound.
No kernel may reach another device: no remote copies, remote signals or barrier semaphores. Data moves between devices by JAX's collectives and lax.ppermute only.
A program may use at most 64 MiB of HBM per device.

```python
import math
import jax
import jax.numpy as jnp
import numpy as np
from jax import lax

D = 4096
HEADS = 32
KV_HEADS = 2
HEAD = 128
HID = 1024
TOP = 8
STEPS = 2
ROWS_DEV = 16
CACHE = 512
EXPERTS = 64
ROWS = 1024
ATT_ROWS = 2
MOST = 3
N_DP = 64
N_MP = 8


def attention_draw(key):
    key_list = jax.random.split(jax.random.fold_in(key, 11), 3)
    group_size = HEADS // KV_HEADS
    fresh_keys = jax.random.normal(key_list[0], (STEPS, ROWS, KV_HEADS, HEAD), jnp.float32)
    query_noise = jax.random.normal(key_list[1], (STEPS, ROWS, HEADS, HEAD), jnp.float32)
    cached = jax.random.normal(key_list[2], (ROWS, CACHE, KV_HEADS, HEAD), jnp.float32)
    queried = 0.35 * jnp.repeat(fresh_keys, group_size, axis=2) + query_noise
    return (queried, fresh_keys, cached)


def draw_queries(key, part):
    return attention_draw(key)[0].astype(jnp.bfloat16)


def draw_new_keys(key, part):
    return attention_draw(key)[1].astype(jnp.bfloat16)


def draw_cache_keys(key, part):
    return attention_draw(key)[2].astype(jnp.bfloat16)


def draw_x_in(key, part):
    key_list = jax.random.split(jax.random.fold_in(key, 31), 4)
    row_scale = jnp.exp(jax.random.uniform(key_list[0], (STEPS, ROWS, 1), jnp.float32, math.log(0.3), math.log(3.0)))
    col_scale = jnp.exp(jax.random.uniform(key_list[1], (D,), jnp.float32, math.log(0.3), math.log(3.0)))
    values = jax.random.normal(key_list[3], (STEPS, ROWS, D), jnp.float32) * row_scale * col_scale
    return values.astype(jnp.bfloat16)


def draw_router(key, part):
    key_list = jax.random.split(jax.random.fold_in(key, 41), 2)
    values = jax.random.normal(key_list[0], (D, EXPERTS), jnp.float32)
    col_scale = jnp.exp(jax.random.uniform(key_list[1], (EXPERTS,), jnp.float32, math.log(0.5), math.log(4.0)))
    return (values * col_scale / math.sqrt(D)).astype(jnp.bfloat16)


def draw_lengths(key, part):
    key_list = jax.random.split(jax.random.fold_in(key, 53), 2)
    random_length = jax.random.randint(key_list[0], (ROWS,), CACHE // 8, CACHE + 1)
    full_at = jax.random.randint(key_list[1], (ROWS // ATT_ROWS,), 0, ATT_ROWS)
    position = jnp.arange(ROWS) % ATT_ROWS
    return jnp.where(position == jnp.repeat(full_at, ATT_ROWS), CACHE, random_length).astype(jnp.int32)


def levels(stream_key, dims, cuts, smallest, high):
    def one(axis_at, shards_of):
        heights = jax.random.uniform(jax.random.fold_in(jax.random.fold_in(stream_key, 6), axis_at), (shards_of,), jnp.float32, smallest / len(cuts), high / len(cuts))
        return jnp.repeat(jnp.exp(heights), dims[axis_at] // shards_of).reshape((-1,) + (1,) * (len(dims) - axis_at - 1))

    level = one(*cuts[0])
    for cut in cuts[1:]:
        level = level * one(*cut)
    return level


def shared_out(key, own, number, rows, amount, top, limit, lean):
    sequence = jax.random.permutation(key, amount)
    heavy_load, common = shares(amount, rows * top, limit, lean, True), shares(amount, rows * top, limit, lean, False)
    places = jnp.arange(amount)

    def named(sizes, offset_by):
        used = int((sizes > 0).sum())
        fixed = max(1, used // 4)
        shifted = fixed + (places - fixed + offset_by * (used - fixed)) % max(1, amount - fixed)
        return jnp.zeros((amount,), jnp.int32).at[sequence[jnp.where(places < fixed, places, shifted)]].set(jnp.asarray(sizes, jnp.int32))

    sizes = jnp.where(number % 4 == 0, named(heavy_load, number // 4), named(common, number - number // 4 - 1))
    mixed = jax.random.permutation(jax.random.fold_in(own, 3), amount)
    donor, receiver = mixed[0:amount // 2 * 2:2], mixed[1:amount // 2 * 2:2]
    room = jnp.minimum(sizes[donor] - 1, limit - sizes[receiver]) // 2
    room = jnp.where((donor == sequence[0]) | (receiver == sequence[0]) | (sizes[receiver] == 0), 0, jnp.maximum(room, 0))
    shifted = jax.random.randint(jax.random.fold_in(own, 4), (amount // 2,), 0, 1 << 20) % (room + 1)
    sizes = sizes.at[donor].add(-shifted).at[receiver].add(shifted)
    labels = jnp.searchsorted(jnp.cumsum(sizes), jnp.arange(rows * top), side="right").astype(jnp.int32)
    grid = labels.reshape(top, rows).T
    grid = grid[jax.random.permutation(jax.random.fold_in(own, 1), rows)]
    offset_by = jax.random.randint(jax.random.fold_in(own, 2), (rows, 1), 0, top)
    return jnp.take_along_axis(grid, (jnp.arange(top)[None, :] + offset_by) % top, axis=1)


def shares(amount, total, limit, skew, full):
    loads = [(1 << 20) // math.isqrt(standing ** skew) + 1 for standing in range(1, amount + 1)]
    largest = limit if full else min(limit, max(-(-total // amount), total * loads[0] // sum(loads)))
    least = 1 if total - largest >= amount - 1 else 0
    counts, spare = [largest] + [least] * (amount - 1), total - largest - least * (amount - 1)
    while spare > 0:
        free = [i for i in range(1, amount) if counts[i] < largest] or [i for i in range(1, amount) if counts[i] < limit]
        mass, budget = sum([loads[i] for i in free]), spare
        for i in free:
            addition = min(limit - counts[i], max(1, budget * loads[i] // mass), spare)
            counts[i] = counts[i] + addition
            spare = spare - addition
    return np.array(counts)


def normal_values(stream_key, dims, scale, limit, shards=(), held_as=jnp.bfloat16):
    array = scale * jax.random.normal(stream_key, dims, jnp.float32)
    if shards:
        array = array * levels(stream_key, dims, shards, -0.22, 0.18)
    return jnp.clip(array, -limit, limit).astype(held_as)


def setup_inputs(seed: int = 0) -> dict:
    seeds = jax.random.split(jax.random.key(seed), 13)
    x_in = draw_x_in(jax.random.fold_in(seeds[12], 71), 0)
    queries = draw_queries(jax.random.fold_in(seeds[12], 71), 0)
    new_keys = draw_new_keys(jax.random.fold_in(seeds[12], 71), 0)
    new_values = normal_values(seeds[3], (STEPS, ROWS, KV_HEADS, HEAD), 1.0, 6.0, ((1, 512),))
    cache_keys = draw_cache_keys(jax.random.fold_in(seeds[12], 71), 0)
    cache_values = normal_values(seeds[5], (ROWS, CACHE, KV_HEADS, HEAD), 1.0, 6.0, ((0, 512),))
    lengths = draw_lengths(jax.random.fold_in(seeds[12], 71), 0)
    o_weight = normal_values(seeds[7], (HEADS * HEAD, D), (HEADS * HEAD // 16) ** -0.5, 0.375, ((0, 8), (1, 64)))
    norm_gain = jnp.clip(1.0 + 0.18 * jax.random.normal(seeds[8], (D,), jnp.float32), 0.1, 1.9)
    router = draw_router(jax.random.fold_in(seeds[12], 71), 0)
    routes_keys = jax.random.split(jax.random.fold_in(seeds[10], 1), STEPS * ROWS // ROWS_DEV)
    routes_turns = jax.random.permutation(jax.random.fold_in(seeds[10], 3), STEPS * ROWS // ROWS_DEV)
    routes = jax.vmap(lambda own, number: shared_out(jax.random.fold_in(seeds[10], 2), own, number, ROWS_DEV, EXPERTS, TOP, MOST, 2))(routes_keys, routes_turns).reshape((STEPS, ROWS, TOP))
    expert_shards = normal_values(seeds[11], (3, EXPERTS, D, HID), (D // 4) ** -0.5, 0.1875, ((2, 512),))
    return {"x_in": x_in, "queries": queries, "new_keys": new_keys, "new_values": new_values, "cache_keys": cache_keys, "cache_values": cache_values, "lengths": lengths, "o_weight": o_weight, "norm_gain": norm_gain, "router": router, "routes": routes, "expert_shards": expert_shards}


def attend(queries, new_keys, new_values, cache_keys, cache_values, lengths):
    steps, att_rows, heads, head_width = queries.shape
    kv_count = new_keys.shape[2]
    cache_len = cache_keys.shape[1]
    scaling = 1.0 / head_width ** 0.5
    grouped = queries.astype(jnp.float32).reshape(steps, att_rows, kv_count, heads // kv_count, head_width)
    past = jnp.einsum('sbkgd,blkd->sbkgl', grouped, cache_keys.astype(jnp.float32)) * scaling
    fresh = jnp.einsum('sbkgd,tbkd->sbkgt', grouped, new_keys.astype(jnp.float32)) * scaling
    present = jnp.arange(cache_len)[None, :] < lengths[:, None]
    past = jnp.where(present[None, :, None, None, :], past, -1e+30)
    earlier = jnp.arange(steps)[None, :] <= jnp.arange(steps)[:, None]
    fresh = jnp.where(earlier[:, None, None, None, :], fresh, -1e+30)
    highest = jnp.maximum(lax.optimization_barrier(jnp.max(past, axis=-1)), lax.optimization_barrier(jnp.max(fresh, axis=-1)))[..., None]
    past_exp = jnp.exp(past - highest)
    fresh_exp = jnp.exp(fresh - highest)
    totals = lax.optimization_barrier(jnp.sum(past_exp, axis=-1, keepdims=True)) + lax.optimization_barrier(jnp.sum(fresh_exp, axis=-1, keepdims=True))
    past_prob = (past_exp / totals).astype(jnp.bfloat16).astype(jnp.float32)
    fresh_prob = (fresh_exp / totals).astype(jnp.bfloat16).astype(jnp.float32)
    mixed = jnp.einsum('sbkgl,blkd->sbkgd', past_prob, cache_values.astype(jnp.float32))
    mixed = mixed + jnp.einsum('sbkgt,tbkd->sbkgd', fresh_prob, new_values.astype(jnp.float32))
    return mixed.astype(jnp.bfloat16).reshape(steps, att_rows, heads * head_width)

def block_attend(pieces):
    return attend(*pieces)

def reference(x_in, queries, new_keys, new_values, cache_keys, cache_values, lengths, o_weight, norm_gain, router, routes, expert_shards):
    query_blocks = queries.reshape(STEPS, N_DP, ROWS_DEV, HEADS, HEAD).transpose(1, 0, 2, 3, 4)
    key_blocks = new_keys.reshape(STEPS, N_DP, ROWS_DEV, KV_HEADS, HEAD).transpose(1, 0, 2, 3, 4)
    value_blocks = new_values.reshape(STEPS, N_DP, ROWS_DEV, KV_HEADS, HEAD).transpose(1, 0, 2, 3, 4)
    cached_keys = cache_keys.reshape(N_DP, ROWS_DEV, CACHE, KV_HEADS, HEAD)
    cached_values = cache_values.reshape(N_DP, ROWS_DEV, CACHE, KV_HEADS, HEAD)
    length_blocks = lengths.reshape(N_DP, ROWS_DEV)
    attended = lax.map(block_attend, (query_blocks, key_blocks, value_blocks, cached_keys, cached_values, length_blocks))
    attended = attended.transpose(1, 0, 2, 3).reshape(STEPS * ROWS, HEADS * HEAD)
    attn_out = jnp.dot(attended, o_weight, preferred_element_type=jnp.float32)
    resid = (x_in.reshape(STEPS * ROWS, D).astype(jnp.float32) + attn_out).astype(jnp.bfloat16)
    resid_f = resid.astype(jnp.float32)
    stat = lax.optimization_barrier(jnp.mean(resid_f * resid_f, axis=-1, keepdims=True))
    normed = (resid_f * lax.rsqrt(stat + 1e-06) * norm_gain).astype(jnp.bfloat16)
    logits = jnp.dot(normed, router, preferred_element_type=jnp.float32)
    expert_ids = routes.reshape(STEPS * ROWS, TOP)
    chosen = jnp.take_along_axis(logits, expert_ids, axis=1)
    gates = jax.nn.softmax(chosen, axis=-1).astype(jnp.bfloat16)
    gate_flat = gates.reshape(-1).astype(jnp.float32)
    id_flat = expert_ids.reshape(-1)
    bound = STEPS * N_DP * MOST
    group_width = HID // N_MP

    def per_expert(carry, expert):
        hit = id_flat == expert
        count = jnp.sum(hit.astype(jnp.int32))
        picked = jnp.nonzero(hit, size=bound, fill_value=0)[0]
        live = jnp.arange(bound) < count
        row_index = picked // TOP
        inputs = normed[row_index]
        gate_out = jnp.dot(inputs, expert_shards[0, expert], preferred_element_type=jnp.float32)
        up_out = jnp.dot(inputs, expert_shards[1, expert], preferred_element_type=jnp.float32)
        hidden = (jax.nn.silu(gate_out) * up_out).astype(jnp.bfloat16)
        down_t = expert_shards[2, expert]
        total = jnp.zeros((bound, D), jnp.float32)
        for group in range(N_MP):
            lower = group * group_width
            piece = jnp.dot(hidden[:, lower:lower + group_width], down_t[:, lower:lower + group_width].T, preferred_element_type=jnp.float32).astype(jnp.bfloat16)
            piece = lax.optimization_barrier(piece)
            total = total + piece.astype(jnp.float32)
        weight = jnp.where(live, gate_flat[picked], 0.0)
        carry = carry.at[row_index].add(weight[:, None] * total)
        return (carry, None)
    moe, _ = lax.scan(per_expert, jnp.zeros((STEPS * ROWS, D), jnp.float32), jnp.arange(EXPERTS))
    mixed_out = (resid.astype(jnp.float32) + moe).astype(jnp.bfloat16)
    return mixed_out.reshape(STEPS, ROWS, D)
```

```python
import math

import jax
import jax.numpy as jnp
from jax import lax
from jax.sharding import PartitionSpec as P


def attend(queries, new_keys, new_values, cache_keys, cache_values, lengths):
    steps, att_rows, heads, head_width = queries.shape
    kv_count = new_keys.shape[2]
    cache_len = cache_keys.shape[1]
    scaling = 1.0 / math.sqrt(head_width)
    grouped = queries.reshape(steps, att_rows, kv_count, heads // kv_count, head_width)
    past = (
        jnp.einsum("sbkgd,blkd->sbkgl", grouped, cache_keys, preferred_element_type=jnp.float32)
        * scaling
    )
    fresh = (
        jnp.einsum("sbkgd,tbkd->sbkgt", grouped, new_keys, preferred_element_type=jnp.float32)
        * scaling
    )
    present = lax.broadcasted_iota(jnp.int32, (att_rows, cache_len), 1) < lengths[:, None]
    past = jnp.where(present[None, :, None, None, :], past, -1e30)
    earlier = lax.broadcasted_iota(jnp.int32, (steps, steps), 1) <= lax.broadcasted_iota(
        jnp.int32, (steps, steps), 0
    )
    fresh = jnp.where(earlier[:, None, None, None, :], fresh, -1e30)
    highest = jnp.maximum(jnp.max(past, axis=-1), jnp.max(fresh, axis=-1))[..., None]
    past_exp = jnp.exp(past - highest)
    fresh_exp = jnp.exp(fresh - highest)
    totals = jnp.sum(past_exp, axis=-1, keepdims=True) + jnp.sum(fresh_exp, axis=-1, keepdims=True)
    past_prob = (past_exp / totals).astype(jnp.bfloat16)
    fresh_prob = (fresh_exp / totals).astype(jnp.bfloat16)
    mixed = jnp.einsum(
        "sbkgl,blkd->sbkgd", past_prob, cache_values, preferred_element_type=jnp.float32
    )
    mixed = mixed + jnp.einsum(
        "sbkgt,tbkd->sbkgd", fresh_prob, new_values, preferred_element_type=jnp.float32
    )
    return mixed.astype(jnp.bfloat16).reshape(steps, att_rows, heads * head_width)


def shards(
    x_in,
    queries,
    new_keys,
    new_values,
    cache_keys,
    cache_values,
    lengths,
    o_weight,
    norm_gain,
    router,
    routes,
    expert_shards,
):
    dp_count = lax.axis_size("dp")
    mp_count = lax.axis_size("mp")
    steps, rows_dev, features = x_in.shape
    expert_total = router.shape[1]
    top_count = routes.shape[2]
    per_step_most = 3 * rows_dev * top_count // (2 * expert_total)
    capacity = steps * per_step_most
    shard_rows = features // (dp_count * mp_count)
    paired_rows = steps * rows_dev
    slot_total = expert_total * capacity
    column_share = features // mp_count
    share_start = lax.axis_index("mp") * column_share
    relaid = lax.all_to_all(
        lax.all_to_all(expert_shards, "dp", split_axis=1, concat_axis=2, tiled=True),
        "mp",
        split_axis=3,
        concat_axis=2,
        tiled=True,
    )
    attended = attend(queries, new_keys, new_values, cache_keys, cache_values, lengths)
    head_share = lax.all_to_all(attended, "mp", split_axis=2, concat_axis=1, tiled=True)
    every_row = lax.all_gather(head_share, "dp", axis=1, tiled=True)
    local_cols = jnp.einsum("srh,hd->srd", every_row, o_weight, preferred_element_type=jnp.float32)
    own_rows = lax.all_to_all(local_cols, "dp", split_axis=1, concat_axis=2, tiled=True)
    partial_out = own_rows.reshape(paired_rows, mp_count, column_share)
    share_parts = lax.all_to_all(partial_out, "mp", split_axis=1, concat_axis=1, tiled=True)
    attn_share = jnp.sum(share_parts, axis=1)
    x_share = lax.dynamic_slice_in_dim(
        x_in.reshape(paired_rows, features), share_start, column_share, 1
    )
    resid_share = (x_share.astype(jnp.float32) + attn_share).astype(jnp.bfloat16)
    resid = lax.all_to_all(
        jnp.broadcast_to(resid_share[:, None, :], (paired_rows, mp_count, column_share)),
        "mp",
        split_axis=1,
        concat_axis=1,
        tiled=True,
    ).reshape(paired_rows, features)
    resid_f = resid.astype(jnp.float32)
    stat = jnp.mean(resid_f * resid_f, axis=-1, keepdims=True)
    normed = (resid_f * lax.rsqrt(stat + 1e-06) * norm_gain).astype(jnp.bfloat16)
    logits = jnp.dot(normed, router, preferred_element_type=jnp.float32)
    expert_ids = routes.reshape(paired_rows, top_count)
    id_match = expert_ids[:, :, None] == lax.broadcasted_iota(jnp.int32, (1, 1, expert_total), 2)
    chosen = jnp.sum(jnp.where(id_match, logits[:, None, :], 0.0), axis=2)
    gates = jax.nn.softmax(chosen, axis=-1).astype(jnp.bfloat16)
    row_counts = jnp.sum(id_match.astype(jnp.int32), axis=1).reshape(steps, rows_dev, expert_total)
    before_count = (jnp.cumsum(row_counts, axis=1) - row_counts).reshape(
        paired_rows, 1, expert_total
    )
    rank_in_step = jnp.sum(jnp.where(id_match, before_count, 0), axis=2)
    step_index = lax.broadcasted_iota(jnp.int32, (steps, rows_dev, top_count), 0).reshape(
        paired_rows, top_count
    )
    target_slot = expert_ids * capacity + step_index * per_step_most + rank_in_step
    slot_match = target_slot[:, :, None] == lax.broadcasted_iota(jnp.int32, (1, 1, slot_total), 2)
    spread_rows = jnp.any(slot_match, axis=1).astype(jnp.bfloat16)
    weigh_slots = jnp.sum(
        jnp.where(slot_match, gates[:, :, None].astype(jnp.float32), 0.0), axis=1
    ).astype(jnp.bfloat16)
    reordered = (
        normed.reshape(paired_rows, dp_count, mp_count, shard_rows)
        .transpose(0, 2, 1, 3)
        .reshape(paired_rows, features)
    )
    outgoing = lax.dot_general(
        spread_rows, reordered, (((0,), (0,)), ((), ())), preferred_element_type=jnp.float32
    )
    outgoing = outgoing.astype(jnp.bfloat16).reshape(expert_total, capacity, features)
    arrived = lax.all_to_all(outgoing, "dp", split_axis=0, concat_axis=1, tiled=True)
    produced = []
    gate_out = jnp.dot(arrived[0], relaid[0, 0], preferred_element_type=jnp.float32)
    up_out = jnp.dot(arrived[0], relaid[1, 0], preferred_element_type=jnp.float32)
    hidden = (jax.nn.silu(gate_out) * up_out).astype(jnp.bfloat16)
    down_out = lax.dot_general(
        hidden, relaid[2, 0], (((1,), (1,)), ((), ())), preferred_element_type=jnp.float32
    )
    produced.append(down_out.astype(jnp.bfloat16))
    produced = jnp.stack(produced)
    returned = lax.all_to_all(produced, "dp", split_axis=1, concat_axis=0, tiled=True)
    combined = jnp.dot(
        weigh_slots, returned.reshape(slot_total, features), preferred_element_type=jnp.float32
    )
    shaped = combined.astype(jnp.bfloat16).reshape(
        paired_rows, mp_count, mp_count, dp_count // mp_count, shard_rows
    )
    hidden_parts = lax.all_to_all(shaped, "mp", split_axis=2, concat_axis=2, tiled=True)
    own_share = jnp.sum(hidden_parts.astype(jnp.float32), axis=2)
    moe_share = own_share.transpose(0, 2, 1, 3).reshape(paired_rows, column_share)
    mixed_out = (resid_share.astype(jnp.float32) + moe_share).astype(jnp.bfloat16)
    return mixed_out.reshape(steps, rows_dev, column_share)


def solution(mesh):
    return jax.shard_map(
        shards,
        mesh=mesh,
        in_specs=(
            P(None, "dp", None),
            P(None, ("dp", "mp"), None, None),
            P(None, ("dp", "mp"), None, None),
            P(None, ("dp", "mp"), None, None),
            P(("dp", "mp"), None, None, None),
            P(("dp", "mp"), None, None, None),
            P(("dp", "mp")),
            P("mp", "dp"),
            P(),
            P(),
            P(None, "dp", None),
            P(None, None, ("dp", "mp"), None),
        ),
        out_specs=P(None, "dp", "mp"),
        check_vma=False,
    )
```

```python
import math

import jax
import jax.numpy as jnp
from jax import lax
from jax.sharding import PartitionSpec as P


def attend(queries, new_keys, new_values, cache_keys, cache_values, lengths):
    steps, att_rows, heads, head_width = queries.shape
    kv_count = new_keys.shape[2]
    cache_len = cache_keys.shape[1]
    scaling = 1.0 / math.sqrt(head_width)
    grouped = queries.reshape(steps, att_rows, kv_count, heads // kv_count, head_width)
    past = (
        jnp.einsum("sbkgd,blkd->sbkgl", grouped, cache_keys, preferred_element_type=jnp.float32)
        * scaling
    )
    fresh = (
        jnp.einsum("sbkgd,tbkd->sbkgt", grouped, new_keys, preferred_element_type=jnp.float32)
        * scaling
    )
    present = lax.broadcasted_iota(jnp.int32, (att_rows, cache_len), 1) < lengths[:, None]
    past = jnp.where(present[None, :, None, None, :], past, -1e30)
    earlier = lax.broadcasted_iota(jnp.int32, (steps, steps), 1) <= lax.broadcasted_iota(
        jnp.int32, (steps, steps), 0
    )
    fresh = jnp.where(earlier[:, None, None, None, :], fresh, -1e30)
    highest = jnp.maximum(jnp.max(past, axis=-1), jnp.max(fresh, axis=-1))[..., None]
    past_exp = jnp.exp(past - highest)
    fresh_exp = jnp.exp(fresh - highest)
    totals = jnp.sum(past_exp, axis=-1, keepdims=True) + jnp.sum(fresh_exp, axis=-1, keepdims=True)
    past_prob = (past_exp / totals).astype(jnp.bfloat16)
    fresh_prob = (fresh_exp / totals).astype(jnp.bfloat16)
    mixed = jnp.einsum(
        "sbkgl,blkd->sbkgd", past_prob, cache_values, preferred_element_type=jnp.float32
    )
    mixed = mixed + jnp.einsum(
        "sbkgt,tbkd->sbkgd", fresh_prob, new_values, preferred_element_type=jnp.float32
    )
    return mixed.astype(jnp.bfloat16).reshape(steps, att_rows, heads * head_width)


def shards(
    x_in,
    queries,
    new_keys,
    new_values,
    cache_keys,
    cache_values,
    lengths,
    o_weight,
    norm_gain,
    router,
    routes,
    expert_shards,
):
    dp_count = lax.axis_size("dp")
    mp_count = lax.axis_size("mp")
    steps, rows_dev, features = x_in.shape
    expert_total = router.shape[1]
    top_count = routes.shape[2]
    per_step_most = 3 * rows_dev * top_count // (2 * expert_total)
    capacity = steps * per_step_most
    shard_rows = features // (dp_count * mp_count)
    paired_rows = steps * rows_dev
    slot_total = expert_total * capacity
    column_share = features // mp_count
    share_start = lax.axis_index("mp") * column_share
    hid_group = expert_shards.shape[3] // mp_count
    weight_blocks = (
        expert_shards.reshape(3, expert_total, shard_rows, mp_count, hid_group)
        .transpose(1, 3, 0, 2, 4)
        .reshape(expert_total * mp_count, 3, shard_rows, hid_group)
    )
    relaid = lax.all_to_all(
        weight_blocks, ("dp", "mp"), split_axis=0, concat_axis=0, tiled=True
    )
    relaid = relaid.transpose(1, 0, 2, 3).reshape(3, 1, features, hid_group)
    attended = attend(queries, new_keys, new_values, cache_keys, cache_values, lengths)
    head_share = lax.all_to_all(attended, "mp", split_axis=2, concat_axis=1, tiled=True)
    every_row = lax.all_gather(head_share, "dp", axis=1, tiled=True)
    every_row, relaid = lax.optimization_barrier((every_row, relaid))
    local_cols = jnp.einsum("srh,hd->srd", every_row, o_weight, preferred_element_type=jnp.float32)
    own_rows = lax.all_to_all(local_cols, "dp", split_axis=1, concat_axis=2, tiled=True)
    partial_out = own_rows.reshape(paired_rows, mp_count, column_share)
    share_parts = lax.all_to_all(partial_out, "mp", split_axis=1, concat_axis=1, tiled=True)
    attn_share = jnp.sum(share_parts, axis=1)
    x_share = lax.dynamic_slice_in_dim(
        x_in.reshape(paired_rows, features), share_start, column_share, 1
    )
    resid_share = (x_share.astype(jnp.float32) + attn_share).astype(jnp.bfloat16)
    resid = lax.all_to_all(
        jnp.broadcast_to(resid_share[:, None, :], (paired_rows, mp_count, column_share)),
        "mp",
        split_axis=1,
        concat_axis=1,
        tiled=True,
    ).reshape(paired_rows, features)
    resid_f = resid.astype(jnp.float32)
    stat = jnp.mean(resid_f * resid_f, axis=-1, keepdims=True)
    normed = (resid_f * lax.rsqrt(stat + 1e-06) * norm_gain).astype(jnp.bfloat16)
    logits = jnp.dot(normed, router, preferred_element_type=jnp.float32)
    expert_ids = routes.reshape(paired_rows, top_count)
    id_match = expert_ids[:, :, None] == lax.broadcasted_iota(jnp.int32, (1, 1, expert_total), 2)
    chosen = jnp.sum(jnp.where(id_match, logits[:, None, :], 0.0), axis=2)
    gates = jax.nn.softmax(chosen, axis=-1).astype(jnp.bfloat16)
    row_counts = jnp.sum(id_match.astype(jnp.int32), axis=1).reshape(steps, rows_dev, expert_total)
    before_count = (jnp.cumsum(row_counts, axis=1) - row_counts).reshape(
        paired_rows, 1, expert_total
    )
    rank_in_step = jnp.sum(jnp.where(id_match, before_count, 0), axis=2)
    step_index = lax.broadcasted_iota(jnp.int32, (steps, rows_dev, top_count), 0).reshape(
        paired_rows, top_count
    )
    target_slot = expert_ids * capacity + step_index * per_step_most + rank_in_step
    slot_match = target_slot[:, :, None] == lax.broadcasted_iota(jnp.int32, (1, 1, slot_total), 2)
    spread_rows = jnp.any(slot_match, axis=1).astype(jnp.bfloat16)
    weigh_slots = jnp.sum(
        jnp.where(slot_match, gates[:, :, None].astype(jnp.float32), 0.0), axis=1
    ).astype(jnp.bfloat16)
    outgoing = lax.dot_general(
        spread_rows, normed, (((0,), (0,)), ((), ())), preferred_element_type=jnp.float32
    )
    outgoing = outgoing.astype(jnp.bfloat16).reshape(expert_total, capacity, features)
    arrived = lax.all_to_all(outgoing, "dp", split_axis=0, concat_axis=1, tiled=True)
    produced = []
    gate_out = jnp.dot(arrived[0], relaid[0, 0], preferred_element_type=jnp.float32)
    up_out = jnp.dot(arrived[0], relaid[1, 0], preferred_element_type=jnp.float32)
    hidden = (jax.nn.silu(gate_out) * up_out).astype(jnp.bfloat16)
    down_out = lax.dot_general(
        hidden, relaid[2, 0], (((1,), (1,)), ((), ())), preferred_element_type=jnp.float32
    )
    produced.append(down_out.astype(jnp.bfloat16))
    produced = jnp.stack(produced)
    returned = lax.all_to_all(produced, "dp", split_axis=1, concat_axis=0, tiled=True)
    combined = jnp.dot(
        weigh_slots, returned.reshape(slot_total, features), preferred_element_type=jnp.float32
    )
    shaped = combined.astype(jnp.bfloat16).reshape(paired_rows, mp_count, column_share)
    hidden_parts = lax.all_to_all(shaped, "mp", split_axis=1, concat_axis=1, tiled=True)
    moe_share = jnp.sum(hidden_parts.astype(jnp.float32), axis=1)
    mixed_out = (resid_share.astype(jnp.float32) + moe_share).astype(jnp.bfloat16)
    return mixed_out.reshape(steps, rows_dev, column_share)


def solution(mesh):
    return jax.shard_map(
        shards,
        mesh=mesh,
        in_specs=(
            P(None, "dp", None),
            P(None, ("dp", "mp"), None, None),
            P(None, ("dp", "mp"), None, None),
            P(None, ("dp", "mp"), None, None),
            P(("dp", "mp"), None, None, None),
            P(("dp", "mp"), None, None, None),
            P(("dp", "mp")),
            P("mp", "dp"),
            P(),
            P(),
            P(None, "dp", None),
            P(None, None, ("dp", "mp"), None),
        ),
        out_specs=P(None, "dp", "mp"),
        check_vma=False,
    )
```

```python
import math

import jax
import jax.numpy as jnp
from jax import lax
from jax.sharding import PartitionSpec as P


def attend(queries, new_keys, new_values, cache_keys, cache_values, lengths):
    steps, att_rows, heads, head_width = queries.shape
    kv_count = new_keys.shape[2]
    cache_len = cache_keys.shape[1]
    scaling = 1.0 / math.sqrt(head_width)
    grouped = queries.reshape(steps, att_rows, kv_count, heads // kv_count, head_width)
    past = (
        jnp.einsum("sbkgd,blkd->sbkgl", grouped, cache_keys, preferred_element_type=jnp.float32)
        * scaling
    )
    fresh = (
        jnp.einsum("sbkgd,tbkd->sbkgt", grouped, new_keys, preferred_element_type=jnp.float32)
        * scaling
    )
    present = lax.broadcasted_iota(jnp.int32, (att_rows, cache_len), 1) < lengths[:, None]
    past = jnp.where(present[None, :, None, None, :], past, -1e30)
    earlier = lax.broadcasted_iota(jnp.int32, (steps, steps), 1) <= lax.broadcasted_iota(
        jnp.int32, (steps, steps), 0
    )
    fresh = jnp.where(earlier[:, None, None, None, :], fresh, -1e30)
    highest = jnp.maximum(jnp.max(past, axis=-1), jnp.max(fresh, axis=-1))[..., None]
    past_exp = jnp.exp(past - highest)
    fresh_exp = jnp.exp(fresh - highest)
    totals = jnp.sum(past_exp, axis=-1, keepdims=True) + jnp.sum(fresh_exp, axis=-1, keepdims=True)
    past_prob = (past_exp / totals).astype(jnp.bfloat16)
    fresh_prob = (fresh_exp / totals).astype(jnp.bfloat16)
    mixed = jnp.einsum(
        "sbkgl,blkd->sbkgd", past_prob, cache_values, preferred_element_type=jnp.float32
    )
    mixed = mixed + jnp.einsum(
        "sbkgt,tbkd->sbkgd", fresh_prob, new_values, preferred_element_type=jnp.float32
    )
    return mixed.astype(jnp.bfloat16).reshape(steps, att_rows, heads * head_width)


def shards(
    x_in,
    queries,
    new_keys,
    new_values,
    cache_keys,
    cache_values,
    lengths,
    o_weight,
    norm_gain,
    router,
    routes,
    expert_shards,
):
    dp_count = lax.axis_size("dp")
    mp_count = lax.axis_size("mp")
    steps, rows_dev, features = x_in.shape
    expert_total = router.shape[1]
    top_count = routes.shape[2]
    per_step_most = 3 * rows_dev * top_count // (2 * expert_total)
    per_step_slots = -(-per_step_most * steps // 8) * 8 // steps
    capacity = steps * per_step_slots
    shard_rows = features // (dp_count * mp_count)
    paired_rows = steps * rows_dev
    slot_total = expert_total * capacity
    column_share = features // mp_count
    share_start = lax.axis_index("mp") * column_share
    hid_group = expert_shards.shape[3] // mp_count
    weight_blocks = (
        expert_shards.reshape(3, expert_total, shard_rows, mp_count, hid_group)
        .transpose(1, 3, 0, 2, 4)
        .reshape(expert_total * mp_count, 3, shard_rows, hid_group)
    )
    relaid = lax.all_to_all(
        weight_blocks, ("dp", "mp"), split_axis=0, concat_axis=0, tiled=True
    )
    relaid = relaid.transpose(1, 0, 2, 3).reshape(3, 1, features, hid_group)
    attended = attend(queries, new_keys, new_values, cache_keys, cache_values, lengths)
    head_share = lax.all_to_all(attended, "mp", split_axis=2, concat_axis=1, tiled=True)
    every_row = lax.all_gather(head_share, "dp", axis=1, tiled=True)
    every_row, relaid = lax.optimization_barrier((every_row, relaid))
    local_cols = jnp.einsum("srh,hd->srd", every_row, o_weight, preferred_element_type=jnp.float32)
    own_rows = lax.all_to_all(local_cols, "dp", split_axis=1, concat_axis=2, tiled=True)
    partial_out = own_rows.reshape(paired_rows, mp_count, column_share)
    share_parts = lax.all_to_all(partial_out, "mp", split_axis=1, concat_axis=1, tiled=True)
    attn_share = jnp.sum(share_parts, axis=1)
    x_share = lax.dynamic_slice_in_dim(
        x_in.reshape(paired_rows, features), share_start, column_share, 1
    )
    resid_share = (x_share.astype(jnp.float32) + attn_share).astype(jnp.bfloat16)
    resid = lax.all_to_all(
        jnp.broadcast_to(resid_share[:, None, :], (paired_rows, mp_count, column_share)),
        "mp",
        split_axis=1,
        concat_axis=1,
        tiled=True,
    ).reshape(paired_rows, features)
    resid_f = resid.astype(jnp.float32)
    stat = jnp.mean(resid_f * resid_f, axis=-1, keepdims=True)
    normed = (resid_f * lax.rsqrt(stat + 1e-06) * norm_gain).astype(jnp.bfloat16)
    logits = jnp.dot(normed, router, preferred_element_type=jnp.float32)
    expert_ids = routes.reshape(paired_rows, top_count)
    id_match = expert_ids[:, :, None] == lax.broadcasted_iota(jnp.int32, (1, 1, expert_total), 2)
    chosen = jnp.sum(jnp.where(id_match, logits[:, None, :], 0.0), axis=2)
    gates = jax.nn.softmax(chosen, axis=-1).astype(jnp.bfloat16)
    row_counts = jnp.sum(id_match.astype(jnp.int32), axis=1).reshape(steps, rows_dev, expert_total)
    before_count = (jnp.cumsum(row_counts, axis=1) - row_counts).reshape(
        paired_rows, 1, expert_total
    )
    rank_in_step = jnp.sum(jnp.where(id_match, before_count, 0), axis=2)
    step_index = lax.broadcasted_iota(jnp.int32, (steps, rows_dev, top_count), 0).reshape(
        paired_rows, top_count
    )
    target_slot = expert_ids * capacity + step_index * per_step_slots + rank_in_step
    slot_match = target_slot[:, :, None] == lax.broadcasted_iota(jnp.int32, (1, 1, slot_total), 2)
    spread_rows = jnp.any(slot_match, axis=1).astype(jnp.bfloat16)
    weigh_slots = jnp.sum(
        jnp.where(slot_match, gates[:, :, None].astype(jnp.float32), 0.0), axis=1
    ).astype(jnp.bfloat16)
    outgoing = lax.dot_general(
        spread_rows, normed, (((0,), (0,)), ((), ())), preferred_element_type=jnp.float32
    )
    outgoing = outgoing.astype(jnp.bfloat16).reshape(expert_total, capacity, features)
    arrived = lax.all_to_all(outgoing, "dp", split_axis=0, concat_axis=1, tiled=True)
    gate_out = jnp.dot(arrived[0], relaid[0, 0], preferred_element_type=jnp.float32)
    up_out = jnp.dot(arrived[0], relaid[1, 0], preferred_element_type=jnp.float32)
    hidden = (jax.nn.silu(gate_out) * up_out).astype(jnp.bfloat16)
    down_out = lax.dot_general(
        hidden, relaid[2, 0], (((1,), (1,)), ((), ())), preferred_element_type=jnp.float32
    )
    produced = down_out.astype(jnp.bfloat16).reshape(expert_total, capacity, features)
    returned = lax.all_to_all(produced, "dp", split_axis=0, concat_axis=0, tiled=True)
    combined = jnp.dot(
        weigh_slots, returned.reshape(slot_total, features), preferred_element_type=jnp.float32
    )
    shaped = combined.astype(jnp.bfloat16).reshape(paired_rows, mp_count, column_share)
    hidden_parts = lax.all_to_all(shaped, "mp", split_axis=1, concat_axis=1, tiled=True)
    moe_share = jnp.sum(hidden_parts.astype(jnp.float32), axis=1)
    mixed_out = (resid_share.astype(jnp.float32) + moe_share).astype(jnp.bfloat16)
    return mixed_out.reshape(steps, rows_dev, column_share)


def solution(mesh):
    return jax.shard_map(
        shards,
        mesh=mesh,
        in_specs=(
            P(None, "dp", None),
            P(None, ("dp", "mp"), None, None),
            P(None, ("dp", "mp"), None, None),
            P(None, ("dp", "mp"), None, None),
            P(("dp", "mp"), None, None, None),
            P(("dp", "mp"), None, None, None),
            P(("dp", "mp")),
            P("mp", "dp"),
            P(),
            P(),
            P(None, "dp", None),
            P(None, None, ("dp", "mp"), None),
        ),
        out_specs=P(None, "dp", "mp"),
        check_vma=False,
    )
```

```python
import math

import jax
import jax.numpy as jnp
from jax import lax
from jax.sharding import PartitionSpec as P


def attend(queries, new_keys, new_values, cache_keys, cache_values, lengths):
    steps, att_rows, heads, head_width = queries.shape
    kv_count = new_keys.shape[2]
    cache_len = cache_keys.shape[1]
    scaling = 1.0 / math.sqrt(head_width)
    grouped = queries.reshape(steps, att_rows, kv_count, heads // kv_count, head_width)
    past = (
        jnp.einsum("sbkgd,blkd->sbkgl", grouped, cache_keys, preferred_element_type=jnp.float32)
        * scaling
    )
    fresh = (
        jnp.einsum("sbkgd,tbkd->sbkgt", grouped, new_keys, preferred_element_type=jnp.float32)
        * scaling
    )
    present = lax.broadcasted_iota(jnp.int32, (att_rows, cache_len), 1) < lengths[:, None]
    past = jnp.where(present[None, :, None, None, :], past, -1e30)
    earlier = lax.broadcasted_iota(jnp.int32, (steps, steps), 1) <= lax.broadcasted_iota(
        jnp.int32, (steps, steps), 0
    )
    fresh = jnp.where(earlier[:, None, None, None, :], fresh, -1e30)
    highest = jnp.maximum(jnp.max(past, axis=-1), jnp.max(fresh, axis=-1))[..., None]
    past_exp = jnp.exp(past - highest)
    fresh_exp = jnp.exp(fresh - highest)
    totals = jnp.sum(past_exp, axis=-1, keepdims=True) + jnp.sum(fresh_exp, axis=-1, keepdims=True)
    past_prob = (past_exp / totals).astype(jnp.bfloat16)
    fresh_prob = (fresh_exp / totals).astype(jnp.bfloat16)
    mixed = jnp.einsum(
        "sbkgl,blkd->sbkgd", past_prob, cache_values, preferred_element_type=jnp.float32
    )
    mixed = mixed + jnp.einsum(
        "sbkgt,tbkd->sbkgd", fresh_prob, new_values, preferred_element_type=jnp.float32
    )
    return mixed.astype(jnp.bfloat16).reshape(steps, att_rows, heads * head_width)


def shards(
    x_in,
    queries,
    new_keys,
    new_values,
    cache_keys,
    cache_values,
    lengths,
    o_weight,
    norm_gain,
    router,
    routes,
    expert_shards,
):
    dp_count = lax.axis_size("dp")
    mp_count = lax.axis_size("mp")
    steps, rows_dev, features = x_in.shape
    expert_total = router.shape[1]
    top_count = routes.shape[2]
    per_step_most = 3 * rows_dev * top_count // (2 * expert_total)
    per_step_slots = -(-per_step_most * steps // 8) * 8 // steps
    capacity = steps * per_step_slots
    shard_rows = features // (dp_count * mp_count)
    paired_rows = steps * rows_dev
    slot_total = expert_total * capacity
    column_share = features // mp_count
    share_start = lax.axis_index("mp") * column_share
    hid_group = expert_shards.shape[3] // mp_count
    weight_blocks = (
        expert_shards.reshape(3, expert_total, shard_rows, mp_count, hid_group)
        .transpose(1, 3, 0, 2, 4)
        .reshape(expert_total * mp_count, 3, shard_rows, hid_group)
    )
    relaid = lax.all_to_all(
        weight_blocks, ("dp", "mp"), split_axis=0, concat_axis=0, tiled=True
    )
    relaid = relaid.transpose(1, 0, 2, 3).reshape(3, 1, features, hid_group)
    attended = attend(queries, new_keys, new_values, cache_keys, cache_values, lengths)
    head_share = lax.all_to_all(attended, "mp", split_axis=2, concat_axis=1, tiled=True)
    every_row = lax.all_gather(head_share, "dp", axis=1, tiled=True)
    every_row, relaid = lax.optimization_barrier((every_row, relaid))
    local_cols = jnp.einsum("srh,hd->srd", every_row, o_weight, preferred_element_type=jnp.float32)
    own_rows = lax.all_to_all(
        local_cols.astype(jnp.bfloat16), "dp", split_axis=1, concat_axis=2, tiled=True
    )
    partial_out = own_rows.reshape(paired_rows, mp_count, column_share)
    share_parts = lax.all_to_all(partial_out, "mp", split_axis=1, concat_axis=1, tiled=True)
    attn_share = jnp.sum(share_parts.astype(jnp.float32), axis=1)
    x_share = lax.dynamic_slice_in_dim(
        x_in.reshape(paired_rows, features), share_start, column_share, 1
    )
    resid_share = (x_share.astype(jnp.float32) + attn_share).astype(jnp.bfloat16)
    resid = lax.all_to_all(
        jnp.broadcast_to(resid_share[:, None, :], (paired_rows, mp_count, column_share)),
        "mp",
        split_axis=1,
        concat_axis=1,
        tiled=True,
    ).reshape(paired_rows, features)
    resid_f = resid.astype(jnp.float32)
    stat = jnp.mean(resid_f * resid_f, axis=-1, keepdims=True)
    normed = (resid_f * lax.rsqrt(stat + 1e-06) * norm_gain).astype(jnp.bfloat16)
    logits = jnp.dot(normed, router, preferred_element_type=jnp.float32)
    expert_ids = routes.reshape(paired_rows, top_count)
    id_match = expert_ids[:, :, None] == lax.broadcasted_iota(jnp.int32, (1, 1, expert_total), 2)
    chosen = jnp.sum(jnp.where(id_match, logits[:, None, :], 0.0), axis=2)
    gates = jax.nn.softmax(chosen, axis=-1).astype(jnp.bfloat16)
    row_counts = jnp.sum(id_match.astype(jnp.int32), axis=1).reshape(steps, rows_dev, expert_total)
    before_count = (jnp.cumsum(row_counts, axis=1) - row_counts).reshape(
        paired_rows, 1, expert_total
    )
    rank_in_step = jnp.sum(jnp.where(id_match, before_count, 0), axis=2)
    step_index = lax.broadcasted_iota(jnp.int32, (steps, rows_dev, top_count), 0).reshape(
        paired_rows, top_count
    )
    target_slot = expert_ids * capacity + step_index * per_step_slots + rank_in_step
    slot_match = target_slot[:, :, None] == lax.broadcasted_iota(jnp.int32, (1, 1, slot_total), 2)
    spread_rows = jnp.any(slot_match, axis=1).astype(jnp.bfloat16)
    weigh_slots = jnp.sum(
        jnp.where(slot_match, gates[:, :, None].astype(jnp.float32), 0.0), axis=1
    ).astype(jnp.bfloat16)
    outgoing = lax.dot_general(
        spread_rows, normed, (((0,), (0,)), ((), ())), preferred_element_type=jnp.float32
    )
    outgoing = outgoing.astype(jnp.bfloat16).reshape(expert_total, capacity, features)
    arrived = lax.all_to_all(outgoing, "dp", split_axis=0, concat_axis=1, tiled=True)
    gate_out = jnp.dot(arrived[0], relaid[0, 0], preferred_element_type=jnp.float32)
    up_out = jnp.dot(arrived[0], relaid[1, 0], preferred_element_type=jnp.float32)
    hidden = (jax.nn.silu(gate_out) * up_out).astype(jnp.bfloat16)
    down_out = lax.dot_general(
        hidden, relaid[2, 0], (((1,), (1,)), ((), ())), preferred_element_type=jnp.float32
    )
    produced = down_out.astype(jnp.bfloat16).reshape(expert_total, capacity, features)
    returned = lax.all_to_all(produced, "dp", split_axis=0, concat_axis=0, tiled=True)
    combined = jnp.dot(
        weigh_slots, returned.reshape(slot_total, features), preferred_element_type=jnp.float32
    )
    shaped = combined.astype(jnp.bfloat16).reshape(paired_rows, mp_count, column_share)
    hidden_parts = lax.all_to_all(shaped, "mp", split_axis=1, concat_axis=1, tiled=True)
    moe_share = jnp.sum(hidden_parts.astype(jnp.float32), axis=1)
    mixed_out = (resid_share.astype(jnp.float32) + moe_share).astype(jnp.bfloat16)
    return mixed_out.reshape(steps, rows_dev, column_share)


def solution(mesh):
    return jax.shard_map(
        shards,
        mesh=mesh,
        in_specs=(
            P(None, "dp", None),
            P(None, ("dp", "mp"), None, None),
            P(None, ("dp", "mp"), None, None),
            P(None, ("dp", "mp"), None, None),
            P(("dp", "mp"), None, None, None),
            P(("dp", "mp"), None, None, None),
            P(("dp", "mp")),
            P("mp", "dp"),
            P(),
            P(),
            P(None, "dp", None),
            P(None, None, ("dp", "mp"), None),
        ),
        out_specs=P(None, "dp", "mp"),
        check_vma=False,
    )
```

```python
import math

import jax
import jax.numpy as jnp
from jax import lax
from jax.sharding import PartitionSpec as P


def attend(queries, new_keys, new_values, cache_keys, cache_values, lengths):
    steps, att_rows, heads, head_width = queries.shape
    kv_count = new_keys.shape[2]
    cache_len = cache_keys.shape[1]
    scaling = 1.0 / math.sqrt(head_width)
    grouped = queries.reshape(steps, att_rows, kv_count, heads // kv_count, head_width)
    past = (
        jnp.einsum("sbkgd,blkd->sbkgl", grouped, cache_keys, preferred_element_type=jnp.float32)
        * scaling
    )
    fresh = (
        jnp.einsum("sbkgd,tbkd->sbkgt", grouped, new_keys, preferred_element_type=jnp.float32)
        * scaling
    )
    present = lax.broadcasted_iota(jnp.int32, (att_rows, cache_len), 1) < lengths[:, None]
    past = jnp.where(present[None, :, None, None, :], past, -1e30)
    earlier = lax.broadcasted_iota(jnp.int32, (steps, steps), 1) <= lax.broadcasted_iota(
        jnp.int32, (steps, steps), 0
    )
    fresh = jnp.where(earlier[:, None, None, None, :], fresh, -1e30)
    highest = jnp.maximum(jnp.max(past, axis=-1), jnp.max(fresh, axis=-1))[..., None]
    past_exp = jnp.exp(past - highest)
    fresh_exp = jnp.exp(fresh - highest)
    totals = jnp.sum(past_exp, axis=-1, keepdims=True) + jnp.sum(fresh_exp, axis=-1, keepdims=True)
    past_prob = (past_exp / totals).astype(jnp.bfloat16)
    fresh_prob = (fresh_exp / totals).astype(jnp.bfloat16)
    mixed = jnp.einsum(
        "sbkgl,blkd->sbkgd", past_prob, cache_values, preferred_element_type=jnp.float32
    )
    mixed = mixed + jnp.einsum(
        "sbkgt,tbkd->sbkgd", fresh_prob, new_values, preferred_element_type=jnp.float32
    )
    return mixed.astype(jnp.bfloat16).reshape(steps, att_rows, heads * head_width)


def shards(
    x_in,
    queries,
    new_keys,
    new_values,
    cache_keys,
    cache_values,
    lengths,
    o_weight,
    norm_gain,
    router,
    routes,
    expert_shards,
):
    mp_count = lax.axis_size("mp")
    steps, rows_dev, features = x_in.shape
    expert_total = router.shape[1]
    top_count = routes.shape[2]
    per_step_most = 3 * rows_dev * top_count // (2 * expert_total)
    per_step_slots = per_step_most
    capacity = steps * per_step_slots
    slot_pack = (capacity // 2, 2)
    shard_rows = expert_shards.shape[2]
    paired_rows = steps * rows_dev
    slot_total = expert_total * capacity
    column_share = features // mp_count
    share_start = lax.axis_index("mp") * column_share
    hid_group = expert_shards.shape[3] // mp_count
    weight_blocks = (
        expert_shards.reshape(3, expert_total, shard_rows, mp_count, hid_group)
        .transpose(1, 3, 0, 2, 4)
        .reshape(expert_total * mp_count, 3, shard_rows, hid_group)
    )
    relaid = lax.all_to_all(
        weight_blocks, ("dy", "dx", "mp"), split_axis=0, concat_axis=0, tiled=True
    )
    relaid = relaid.transpose(1, 0, 2, 3).reshape(3, 1, features, hid_group)
    attended = attend(queries, new_keys, new_values, cache_keys, cache_values, lengths)
    dy_count = lax.axis_size("dy")
    head_pieces = attended.reshape(steps, -1, mp_count, column_share).transpose(2, 0, 1, 3)
    head_pieces = jnp.broadcast_to(head_pieces[None], (dy_count,) + head_pieces.shape)
    head_pieces = head_pieces.reshape((dy_count * mp_count,) + head_pieces.shape[2:])
    row_share = lax.all_to_all(head_pieces, ("dy", "mp"), split_axis=0, concat_axis=0, tiled=True)
    row_share = (
        row_share.reshape((dy_count, mp_count) + row_share.shape[1:])
        .transpose(2, 0, 1, 3, 4)
        .reshape(steps, -1, column_share)
    )
    col_weight = lax.all_gather(o_weight, "dx", axis=1, tiled=True)
    row_share, relaid = lax.optimization_barrier((row_share, relaid))
    local_cols = jnp.einsum(
        "srh,hd->srd", row_share, col_weight, preferred_element_type=jnp.float32
    )
    own_rows = lax.all_to_all(
        local_cols.astype(jnp.bfloat16), "dy", split_axis=1, concat_axis=2, tiled=True
    )
    partial_out = own_rows.reshape(paired_rows, mp_count, column_share)
    share_parts = lax.all_to_all(partial_out, "mp", split_axis=1, concat_axis=1, tiled=True)
    attn_share = jnp.sum(share_parts.astype(jnp.float32), axis=1)
    x_share = lax.dynamic_slice_in_dim(
        x_in.reshape(paired_rows, features), share_start, column_share, 1
    )
    resid_share = (x_share.astype(jnp.float32) + attn_share).astype(jnp.bfloat16)
    resid = lax.all_to_all(
        jnp.broadcast_to(resid_share[:, None, :], (paired_rows, mp_count, column_share)),
        "mp",
        split_axis=1,
        concat_axis=1,
        tiled=True,
    ).reshape(paired_rows, features)
    resid_f = resid.astype(jnp.float32)
    stat = jnp.mean(resid_f * resid_f, axis=-1, keepdims=True)
    normed = (resid_f * lax.rsqrt(stat + 1e-06) * norm_gain).astype(jnp.bfloat16)
    logits = jnp.dot(normed, router, preferred_element_type=jnp.float32)
    expert_ids = routes.reshape(paired_rows, top_count)
    id_match = expert_ids[:, :, None] == lax.broadcasted_iota(jnp.int32, (1, 1, expert_total), 2)
    chosen = jnp.sum(jnp.where(id_match, logits[:, None, :], 0.0), axis=2)
    gates = jax.nn.softmax(chosen, axis=-1).astype(jnp.bfloat16)
    row_counts = jnp.sum(id_match.astype(jnp.int32), axis=1).reshape(steps, rows_dev, expert_total)
    before_count = (jnp.cumsum(row_counts, axis=1) - row_counts).reshape(
        paired_rows, 1, expert_total
    )
    rank_in_step = jnp.sum(jnp.where(id_match, before_count, 0), axis=2)
    step_index = lax.broadcasted_iota(jnp.int32, (steps, rows_dev, top_count), 0).reshape(
        paired_rows, top_count
    )
    target_slot = expert_ids * capacity + step_index * per_step_slots + rank_in_step
    slot_match = target_slot[:, :, None] == lax.broadcasted_iota(jnp.int32, (1, 1, slot_total), 2)
    spread_rows = jnp.any(slot_match, axis=1).astype(jnp.bfloat16)
    weigh_slots = jnp.sum(
        jnp.where(slot_match, gates[:, :, None].astype(jnp.float32), 0.0), axis=1
    ).astype(jnp.bfloat16)
    outgoing = jnp.einsum(
        "rabc,rf->abcf",
        spread_rows.reshape(paired_rows, expert_total, *slot_pack),
        normed,
        preferred_element_type=jnp.float32,
    ).astype(jnp.bfloat16)
    arrived = lax.all_to_all(outgoing, ("dy", "dx"), split_axis=0, concat_axis=0, tiled=True)
    arrived = arrived.reshape(slot_total, features)
    gate_out = jnp.dot(arrived, relaid[0, 0], preferred_element_type=jnp.float32)
    up_out = jnp.dot(arrived, relaid[1, 0], preferred_element_type=jnp.float32)
    hidden = (jax.nn.silu(gate_out) * up_out).astype(jnp.bfloat16)
    down_out = lax.dot_general(
        hidden, relaid[2, 0], (((1,), (1,)), ((), ())), preferred_element_type=jnp.float32
    )
    produced = down_out.astype(jnp.bfloat16).reshape(expert_total, *slot_pack, features)
    returned = lax.all_to_all(produced, ("dy", "dx"), split_axis=0, concat_axis=0, tiled=True)
    combined = jnp.einsum(
        "rabc,abcf->rf",
        weigh_slots.reshape(paired_rows, expert_total, *slot_pack),
        returned,
        preferred_element_type=jnp.float32,
    )
    shaped = combined.astype(jnp.bfloat16).reshape(paired_rows, mp_count, column_share)
    hidden_parts = lax.all_to_all(shaped, "mp", split_axis=1, concat_axis=1, tiled=True)
    moe_share = jnp.sum(hidden_parts.astype(jnp.float32), axis=1)
    mixed_out = (resid_share.astype(jnp.float32) + moe_share).astype(jnp.bfloat16)
    return mixed_out.reshape(steps, rows_dev, column_share)


def solution(mesh):
    inner = 8
    split_mesh = jax.sharding.Mesh(
        mesh.devices.reshape(mesh.shape["dp"] // inner, inner, mesh.shape["mp"]),
        ("dy", "dx", "mp"),
    )
    return jax.shard_map(
        shards,
        mesh=split_mesh,
        in_specs=(
            P(None, ("dy", "dx"), None),
            P(None, ("dy", "dx", "mp"), None, None),
            P(None, ("dy", "dx", "mp"), None, None),
            P(None, ("dy", "dx", "mp"), None, None),
            P(("dy", "dx", "mp"), None, None, None),
            P(("dy", "dx", "mp"), None, None, None),
            P(("dy", "dx", "mp")),
            P("mp", ("dy", "dx")),
            P(),
            P(),
            P(None, ("dy", "dx"), None),
            P(None, None, ("dy", "dx", "mp"), None),
        ),
        out_specs=P(None, ("dy", "dx"), "mp"),
        check_vma=False,
    )
```

```python
import math

import jax
import jax.numpy as jnp
from jax import lax
from jax.sharding import PartitionSpec as P


def attend(queries, new_keys, new_values, cache_keys, cache_values, lengths):
    steps, att_rows, heads, head_width = queries.shape
    kv_count = new_keys.shape[2]
    cache_len = cache_keys.shape[1]
    scaling = 1.0 / math.sqrt(head_width)
    grouped = queries.reshape(steps, att_rows, kv_count, heads // kv_count, head_width)
    past = (
        jnp.einsum("sbkgd,blkd->sbkgl", grouped, cache_keys, preferred_element_type=jnp.float32)
        * scaling
    )
    fresh = (
        jnp.einsum("sbkgd,tbkd->sbkgt", grouped, new_keys, preferred_element_type=jnp.float32)
        * scaling
    )
    present = lax.broadcasted_iota(jnp.int32, (att_rows, cache_len), 1) < lengths[:, None]
    past = jnp.where(present[None, :, None, None, :], past, -1e30)
    earlier = lax.broadcasted_iota(jnp.int32, (steps, steps), 1) <= lax.broadcasted_iota(
        jnp.int32, (steps, steps), 0
    )
    fresh = jnp.where(earlier[:, None, None, None, :], fresh, -1e30)
    highest = jnp.maximum(jnp.max(past, axis=-1), jnp.max(fresh, axis=-1))[..., None]
    past_exp = jnp.exp(past - highest)
    fresh_exp = jnp.exp(fresh - highest)
    totals = jnp.sum(past_exp, axis=-1, keepdims=True) + jnp.sum(fresh_exp, axis=-1, keepdims=True)
    past_prob = (past_exp / totals).astype(jnp.bfloat16)
    fresh_prob = (fresh_exp / totals).astype(jnp.bfloat16)
    mixed = jnp.einsum(
        "sbkgl,blkd->sbkgd", past_prob, cache_values, preferred_element_type=jnp.float32
    )
    mixed = mixed + jnp.einsum(
        "sbkgt,tbkd->sbkgd", fresh_prob, new_values, preferred_element_type=jnp.float32
    )
    return mixed.astype(jnp.bfloat16).reshape(steps, att_rows, heads * head_width)


def shards(
    x_in,
    queries,
    new_keys,
    new_values,
    cache_keys,
    cache_values,
    lengths,
    o_weight,
    norm_gain,
    router,
    routes,
    expert_shards,
):
    mp_count = lax.axis_size("mp")
    steps, rows_dev, features = x_in.shape
    expert_total = router.shape[1]
    top_count = routes.shape[2]
    per_step_most = 3 * rows_dev * top_count // (2 * expert_total)
    per_step_slots = per_step_most
    capacity = steps * per_step_slots
    slot_pack = (capacity // 2, 2)
    shard_rows = expert_shards.shape[2]
    paired_rows = steps * rows_dev
    slot_total = expert_total * capacity
    column_share = features // mp_count
    share_start = lax.axis_index("mp") * column_share
    hid_group = expert_shards.shape[3] // mp_count
    weight_blocks = (
        expert_shards.reshape(3, expert_total, shard_rows, mp_count, hid_group)
        .transpose(1, 3, 0, 2, 4)
        .reshape(expert_total * mp_count, 3, shard_rows, hid_group)
    )
    relaid = lax.all_to_all(
        weight_blocks, ("dy", "dx", "mp"), split_axis=0, concat_axis=0, tiled=True
    )
    attended = attend(queries, new_keys, new_values, cache_keys, cache_values, lengths)
    dy_count = lax.axis_size("dy")
    head_pieces = attended.reshape(steps, -1, mp_count, column_share).transpose(2, 0, 1, 3)
    head_pieces = jnp.broadcast_to(head_pieces[None], (dy_count,) + head_pieces.shape)
    head_pieces = head_pieces.reshape((dy_count * mp_count,) + head_pieces.shape[2:])
    row_share = lax.all_to_all(head_pieces, ("dy", "mp"), split_axis=0, concat_axis=0, tiled=True)
    row_share = (
        row_share.reshape((dy_count, mp_count) + row_share.shape[1:])
        .transpose(2, 0, 1, 3, 4)
        .reshape(steps, -1, column_share)
    )
    col_weight = lax.all_gather(o_weight, "dx", axis=1, tiled=True)
    row_share, relaid = lax.optimization_barrier((row_share, relaid))
    local_cols = jnp.einsum(
        "srh,hd->srd", row_share, col_weight, preferred_element_type=jnp.float32
    )
    own_rows = lax.all_to_all(
        local_cols.astype(jnp.bfloat16), "dy", split_axis=1, concat_axis=2, tiled=True
    )
    partial_out = own_rows.reshape(paired_rows, mp_count, column_share)
    share_parts = lax.all_to_all(partial_out, "mp", split_axis=1, concat_axis=1, tiled=True)
    attn_share = jnp.sum(share_parts.astype(jnp.float32), axis=1)
    x_share = lax.dynamic_slice_in_dim(
        x_in.reshape(paired_rows, features), share_start, column_share, 1
    )
    resid_share = (x_share.astype(jnp.float32) + attn_share).astype(jnp.bfloat16)
    resid = lax.all_to_all(
        jnp.broadcast_to(resid_share[:, None, :], (paired_rows, mp_count, column_share)),
        "mp",
        split_axis=1,
        concat_axis=1,
        tiled=True,
    ).reshape(paired_rows, features)
    resid_f = resid.astype(jnp.float32)
    stat = jnp.mean(resid_f * resid_f, axis=-1, keepdims=True)
    normed = (resid_f * lax.rsqrt(stat + 1e-06) * norm_gain).astype(jnp.bfloat16)
    logits = jnp.dot(normed, router, preferred_element_type=jnp.float32)
    expert_ids = routes.reshape(paired_rows, top_count)
    id_match = expert_ids[:, :, None] == lax.broadcasted_iota(jnp.int32, (1, 1, expert_total), 2)
    chosen = jnp.sum(jnp.where(id_match, logits[:, None, :], 0.0), axis=2)
    gates = jax.nn.softmax(chosen, axis=-1).astype(jnp.bfloat16)
    row_counts = jnp.sum(id_match.astype(jnp.int32), axis=1).reshape(steps, rows_dev, expert_total)
    before_count = (jnp.cumsum(row_counts, axis=1) - row_counts).reshape(
        paired_rows, 1, expert_total
    )
    rank_in_step = jnp.sum(jnp.where(id_match, before_count, 0), axis=2)
    step_index = lax.broadcasted_iota(jnp.int32, (steps, rows_dev, top_count), 0).reshape(
        paired_rows, top_count
    )
    target_slot = expert_ids * capacity + step_index * per_step_slots + rank_in_step
    slot_match = target_slot[:, :, None] == lax.broadcasted_iota(jnp.int32, (1, 1, slot_total), 2)
    spread_rows = jnp.any(slot_match, axis=1).astype(jnp.bfloat16)
    weigh_slots = jnp.sum(
        jnp.where(slot_match, gates[:, :, None].astype(jnp.float32), 0.0), axis=1
    ).astype(jnp.bfloat16)
    outgoing = jnp.einsum(
        "rabc,rf->abcf",
        spread_rows.reshape(paired_rows, expert_total, *slot_pack),
        normed,
        preferred_element_type=jnp.float32,
    ).astype(jnp.bfloat16)
    arrived = lax.all_to_all(outgoing, ("dy", "dx"), split_axis=0, concat_axis=0, tiled=True)
    arrived = arrived.reshape(slot_total, features)
    gate_out = jnp.dot(arrived, relaid[:, 0].reshape(features, hid_group), preferred_element_type=jnp.float32)
    up_out = jnp.dot(arrived, relaid[:, 1].reshape(features, hid_group), preferred_element_type=jnp.float32)
    hidden = (jax.nn.silu(gate_out) * up_out).astype(jnp.bfloat16)
    down_out = lax.dot_general(
        hidden, relaid[:, 2].reshape(features, hid_group), (((1,), (1,)), ((), ())), preferred_element_type=jnp.float32
    )
    produced = down_out.astype(jnp.bfloat16).reshape(expert_total, *slot_pack, features)
    returned = lax.all_to_all(produced, ("dy", "dx"), split_axis=0, concat_axis=0, tiled=True)
    combined = jnp.einsum(
        "rabc,abcf->rf",
        weigh_slots.reshape(paired_rows, expert_total, *slot_pack),
        returned,
        preferred_element_type=jnp.float32,
    )
    shaped = combined.astype(jnp.bfloat16).reshape(paired_rows, mp_count, column_share)
    hidden_parts = lax.all_to_all(shaped, "mp", split_axis=1, concat_axis=1, tiled=True)
    moe_share = jnp.sum(hidden_parts.astype(jnp.float32), axis=1)
    mixed_out = (resid_share.astype(jnp.float32) + moe_share).astype(jnp.bfloat16)
    return mixed_out.reshape(steps, rows_dev, column_share)


def solution(mesh):
    inner = 8
    split_mesh = jax.sharding.Mesh(
        mesh.devices.reshape(mesh.shape["dp"] // inner, inner, mesh.shape["mp"]),
        ("dy", "dx", "mp"),
    )
    return jax.shard_map(
        shards,
        mesh=split_mesh,
        in_specs=(
            P(None, ("dy", "dx"), None),
            P(None, ("dy", "dx", "mp"), None, None),
            P(None, ("dy", "dx", "mp"), None, None),
            P(None, ("dy", "dx", "mp"), None, None),
            P(("dy", "dx", "mp"), None, None, None),
            P(("dy", "dx", "mp"), None, None, None),
            P(("dy", "dx", "mp")),
            P("mp", ("dy", "dx")),
            P(),
            P(),
            P(None, ("dy", "dx"), None),
            P(None, None, ("dy", "dx", "mp"), None),
        ),
        out_specs=P(None, ("dy", "dx"), "mp"),
        check_vma=False,
    )
```

```python
import math

import jax
import jax.numpy as jnp
from jax import lax
from jax.sharding import PartitionSpec as P


def attend(queries, new_keys, new_values, cache_keys, cache_values, lengths):
    steps, att_rows, heads, head_width = queries.shape
    kv_count = new_keys.shape[2]
    cache_len = cache_keys.shape[1]
    scaling = 1.0 / math.sqrt(head_width)
    grouped = queries.reshape(steps, att_rows, kv_count, heads // kv_count, head_width)
    past = (
        jnp.einsum("sbkgd,blkd->sbkgl", grouped, cache_keys, preferred_element_type=jnp.float32)
        * scaling
    )
    fresh = (
        jnp.einsum("sbkgd,tbkd->sbkgt", grouped, new_keys, preferred_element_type=jnp.float32)
        * scaling
    )
    present = lax.broadcasted_iota(jnp.int32, (att_rows, cache_len), 1) < lengths[:, None]
    past = jnp.where(present[None, :, None, None, :], past, -1e30)
    earlier = lax.broadcasted_iota(jnp.int32, (steps, steps), 1) <= lax.broadcasted_iota(
        jnp.int32, (steps, steps), 0
    )
    fresh = jnp.where(earlier[:, None, None, None, :], fresh, -1e30)
    highest = jnp.maximum(jnp.max(past, axis=-1), jnp.max(fresh, axis=-1))[..., None]
    past_exp = jnp.exp(past - highest)
    fresh_exp = jnp.exp(fresh - highest)
    totals = jnp.sum(past_exp, axis=-1, keepdims=True) + jnp.sum(fresh_exp, axis=-1, keepdims=True)
    past_prob = (past_exp / totals).astype(jnp.bfloat16)
    fresh_prob = (fresh_exp / totals).astype(jnp.bfloat16)
    mixed = jnp.einsum(
        "sbkgl,blkd->sbkgd", past_prob, cache_values, preferred_element_type=jnp.float32
    )
    mixed = mixed + jnp.einsum(
        "sbkgt,tbkd->sbkgd", fresh_prob, new_values, preferred_element_type=jnp.float32
    )
    return mixed.astype(jnp.bfloat16).reshape(steps, att_rows, heads * head_width)


def shards(
    x_in,
    queries,
    new_keys,
    new_values,
    cache_keys,
    cache_values,
    lengths,
    o_weight,
    norm_gain,
    router,
    routes,
    expert_shards,
):
    mp_count = lax.axis_size("mp")
    steps, rows_dev, features = x_in.shape
    expert_total = router.shape[1]
    top_count = routes.shape[2]
    per_step_most = 3 * rows_dev * top_count // (2 * expert_total)
    per_step_slots = per_step_most
    capacity = steps * per_step_slots
    slot_pack = (capacity // 2, 2)
    shard_rows = expert_shards.shape[2]
    paired_rows = steps * rows_dev
    slot_total = expert_total * capacity
    column_share = features // mp_count
    share_start = lax.axis_index("mp") * column_share
    hid_group = expert_shards.shape[3] // mp_count
    weight_blocks = (
        expert_shards.reshape(3, expert_total, shard_rows, mp_count, hid_group)
        .transpose(1, 3, 0, 2, 4)
        .reshape(expert_total * mp_count, 3, shard_rows, hid_group)
    )
    relaid = lax.all_to_all(
        weight_blocks, ("dy", "dx", "mp"), split_axis=0, concat_axis=0, tiled=True
    )
    attended = attend(queries, new_keys, new_values, cache_keys, cache_values, lengths)
    dy_count = lax.axis_size("dy")
    head_pieces = attended.reshape(steps, -1, mp_count, column_share).transpose(2, 0, 1, 3)
    head_pieces = jnp.broadcast_to(head_pieces[None], (dy_count,) + head_pieces.shape)
    head_pieces = head_pieces.reshape((dy_count * mp_count,) + head_pieces.shape[2:])
    row_share = lax.all_to_all(head_pieces, ("dy", "mp"), split_axis=0, concat_axis=0, tiled=True)
    row_share = (
        row_share.reshape((dy_count, mp_count) + row_share.shape[1:])
        .transpose(2, 0, 1, 3, 4)
        .reshape(steps, -1, column_share)
    )
    col_weight = lax.all_gather(o_weight, "dx", axis=1, tiled=True)
    row_share, relaid = lax.optimization_barrier((row_share, relaid))
    local_cols = jnp.einsum(
        "srh,hd->srd", row_share, col_weight, preferred_element_type=jnp.float32
    )
    own_rows = lax.all_to_all(
        local_cols.astype(jnp.bfloat16), "dy", split_axis=1, concat_axis=2, tiled=True
    )
    partial_out = own_rows.reshape(paired_rows, mp_count, column_share)
    share_parts = lax.all_to_all(partial_out, "mp", split_axis=1, concat_axis=1, tiled=True)
    attn_share = jnp.sum(share_parts.astype(jnp.float32), axis=1)
    x_share = lax.dynamic_slice_in_dim(
        x_in.reshape(paired_rows, features), share_start, column_share, 1
    )
    resid_share = (x_share.astype(jnp.float32) + attn_share).astype(jnp.bfloat16)
    resid = lax.all_to_all(
        jnp.broadcast_to(resid_share[:, None, :], (paired_rows, mp_count, column_share)),
        "mp",
        split_axis=1,
        concat_axis=1,
        tiled=True,
    ).reshape(paired_rows, features)
    resid_f = resid.astype(jnp.float32)
    stat = jnp.mean(resid_f * resid_f, axis=-1, keepdims=True)
    normed = (resid_f * lax.rsqrt(stat + 1e-06) * norm_gain).astype(jnp.bfloat16)
    logits = jnp.dot(normed, router, preferred_element_type=jnp.float32)
    expert_ids = routes.reshape(paired_rows, top_count)
    id_match = expert_ids[:, :, None] == lax.broadcasted_iota(jnp.int32, (1, 1, expert_total), 2)
    chosen = jnp.sum(jnp.where(id_match, logits[:, None, :], 0.0), axis=2)
    gates = jax.nn.softmax(chosen, axis=-1).astype(jnp.bfloat16)
    row_counts = jnp.sum(id_match.astype(jnp.int32), axis=1).reshape(steps, rows_dev, expert_total)
    before_count = (jnp.cumsum(row_counts, axis=1) - row_counts).reshape(
        paired_rows, 1, expert_total
    )
    rank_in_step = jnp.sum(jnp.where(id_match, before_count, 0), axis=2)
    step_index = lax.broadcasted_iota(jnp.int32, (steps, rows_dev, top_count), 0).reshape(
        paired_rows, top_count
    )
    target_slot = expert_ids * capacity + step_index * per_step_slots + rank_in_step
    slot_match = target_slot[:, :, None] == lax.broadcasted_iota(jnp.int32, (1, 1, slot_total), 2)
    spread_rows = jnp.any(slot_match, axis=1).astype(jnp.bfloat16)
    weigh_slots = jnp.sum(
        jnp.where(slot_match, gates[:, :, None].astype(jnp.float32), 0.0), axis=1
    ).astype(jnp.bfloat16)
    outgoing = jnp.einsum(
        "rabc,rf->abcf",
        spread_rows.reshape(paired_rows, expert_total, *slot_pack),
        normed,
        preferred_element_type=jnp.float32,
    ).astype(jnp.bfloat16)
    arrived = lax.all_to_all(outgoing, ("dy", "dx"), split_axis=0, concat_axis=0, tiled=True)
    gate_out = jnp.einsum(
        "abcf,fh->abch",
        arrived,
        relaid[:, 0].reshape(features, hid_group),
        preferred_element_type=jnp.float32,
    )
    up_out = jnp.einsum(
        "abcf,fh->abch",
        arrived,
        relaid[:, 1].reshape(features, hid_group),
        preferred_element_type=jnp.float32,
    )
    hidden = (jax.nn.silu(gate_out) * up_out).astype(jnp.bfloat16).reshape(slot_total, hid_group)
    down_out = lax.dot_general(
        hidden, relaid[:, 2].reshape(features, hid_group), (((1,), (1,)), ((), ())), preferred_element_type=jnp.float32
    )
    produced = down_out.astype(jnp.bfloat16).reshape(expert_total, *slot_pack, features)
    returned = lax.all_to_all(produced, ("dy", "dx"), split_axis=0, concat_axis=0, tiled=True)
    combined = jnp.einsum(
        "rabc,abcf->rf",
        weigh_slots.reshape(paired_rows, expert_total, *slot_pack),
        returned,
        preferred_element_type=jnp.float32,
    )
    shaped = combined.astype(jnp.bfloat16).reshape(paired_rows, mp_count, column_share)
    hidden_parts = lax.all_to_all(shaped, "mp", split_axis=1, concat_axis=1, tiled=True)
    moe_share = jnp.sum(hidden_parts.astype(jnp.float32), axis=1)
    mixed_out = (resid_share.astype(jnp.float32) + moe_share).astype(jnp.bfloat16)
    return mixed_out.reshape(steps, rows_dev, column_share)


def solution(mesh):
    inner = 8
    split_mesh = jax.sharding.Mesh(
        mesh.devices.reshape(mesh.shape["dp"] // inner, inner, mesh.shape["mp"]),
        ("dy", "dx", "mp"),
    )
    return jax.shard_map(
        shards,
        mesh=split_mesh,
        in_specs=(
            P(None, ("dy", "dx"), None),
            P(None, ("dy", "dx", "mp"), None, None),
            P(None, ("dy", "dx", "mp"), None, None),
            P(None, ("dy", "dx", "mp"), None, None),
            P(("dy", "dx", "mp"), None, None, None),
            P(("dy", "dx", "mp"), None, None, None),
            P(("dy", "dx", "mp")),
            P("mp", ("dy", "dx")),
            P(),
            P(),
            P(None, ("dy", "dx"), None),
            P(None, None, ("dy", "dx", "mp"), None),
        ),
        out_specs=P(None, ("dy", "dx"), "mp"),
        check_vma=False,
    )
```

```python
import math

import jax
import jax.numpy as jnp
from jax import lax
from jax.sharding import PartitionSpec as P


def attend(queries, new_keys, new_values, cache_keys, cache_values, lengths):
    steps, att_rows, heads, head_width = queries.shape
    kv_count = new_keys.shape[2]
    cache_len = cache_keys.shape[1]
    scaling = 1.0 / math.sqrt(head_width)
    grouped = queries.reshape(steps, att_rows, kv_count, heads // kv_count, head_width)
    past = (
        jnp.einsum("sbkgd,blkd->sbkgl", grouped, cache_keys, preferred_element_type=jnp.float32)
        * scaling
    )
    fresh = (
        jnp.einsum("sbkgd,tbkd->sbkgt", grouped, new_keys, preferred_element_type=jnp.float32)
        * scaling
    )
    present = lax.broadcasted_iota(jnp.int32, (att_rows, cache_len), 1) < lengths[:, None]
    past = jnp.where(present[None, :, None, None, :], past, -1e30)
    earlier = lax.broadcasted_iota(jnp.int32, (steps, steps), 1) <= lax.broadcasted_iota(
        jnp.int32, (steps, steps), 0
    )
    fresh = jnp.where(earlier[:, None, None, None, :], fresh, -1e30)
    highest = jnp.maximum(jnp.max(past, axis=-1), jnp.max(fresh, axis=-1))[..., None]
    past_exp = jnp.exp(past - highest)
    fresh_exp = jnp.exp(fresh - highest)
    totals = jnp.sum(past_exp, axis=-1, keepdims=True) + jnp.sum(fresh_exp, axis=-1, keepdims=True)
    past_prob = (past_exp / totals).astype(jnp.bfloat16)
    fresh_prob = (fresh_exp / totals).astype(jnp.bfloat16)
    mixed = jnp.einsum(
        "sbkgl,blkd->sbkgd", past_prob, cache_values, preferred_element_type=jnp.float32
    )
    mixed = mixed + jnp.einsum(
        "sbkgt,tbkd->sbkgd", fresh_prob, new_values, preferred_element_type=jnp.float32
    )
    return mixed.astype(jnp.bfloat16).reshape(steps, att_rows, heads * head_width)


def shards(
    x_in,
    queries,
    new_keys,
    new_values,
    cache_keys,
    cache_values,
    lengths,
    o_weight,
    norm_gain,
    router,
    routes,
    expert_shards,
):
    mp_count = lax.axis_size("mp")
    steps, rows_dev, features = x_in.shape
    expert_total = router.shape[1]
    top_count = routes.shape[2]
    per_step_most = 3 * rows_dev * top_count // (2 * expert_total)
    per_step_slots = per_step_most
    capacity = steps * per_step_slots
    slot_pack = (capacity // 2, 2)
    shard_rows = expert_shards.shape[2]
    paired_rows = steps * rows_dev
    slot_total = expert_total * capacity
    column_share = features // mp_count
    share_start = lax.axis_index("mp") * column_share
    hid_group = expert_shards.shape[3] // mp_count
    weight_blocks = (
        expert_shards.reshape(3, expert_total, shard_rows, mp_count, hid_group)
        .transpose(1, 3, 2, 0, 4)
        .reshape(expert_total * mp_count, shard_rows, 3 * hid_group)
    )
    relaid = lax.all_to_all(
        weight_blocks, ("dy", "dx", "mp"), split_axis=0, concat_axis=0, tiled=True
    )
    attended = attend(queries, new_keys, new_values, cache_keys, cache_values, lengths)
    dy_count = lax.axis_size("dy")
    head_pieces = attended.reshape(steps, -1, mp_count, column_share).transpose(2, 0, 1, 3)
    head_pieces = jnp.broadcast_to(head_pieces[None], (dy_count,) + head_pieces.shape)
    head_pieces = head_pieces.reshape((dy_count * mp_count,) + head_pieces.shape[2:])
    row_share = lax.all_to_all(head_pieces, ("dy", "mp"), split_axis=0, concat_axis=0, tiled=True)
    row_share = (
        row_share.reshape((dy_count, mp_count) + row_share.shape[1:])
        .transpose(2, 0, 1, 3, 4)
        .reshape(steps, -1, column_share)
    )
    col_weight = lax.all_gather(o_weight, "dx", axis=1, tiled=True)
    row_share, relaid = lax.optimization_barrier((row_share, relaid))
    local_cols = jnp.einsum(
        "srh,hd->srd", row_share, col_weight, preferred_element_type=jnp.float32
    )
    own_rows = lax.all_to_all(
        local_cols.astype(jnp.bfloat16), "dy", split_axis=1, concat_axis=2, tiled=True
    )
    partial_out = own_rows.reshape(paired_rows, mp_count, column_share)
    share_parts = lax.all_to_all(partial_out, "mp", split_axis=1, concat_axis=1, tiled=True)
    attn_share = jnp.sum(share_parts.astype(jnp.float32), axis=1)
    x_share = lax.dynamic_slice_in_dim(
        x_in.reshape(paired_rows, features), share_start, column_share, 1
    )
    resid_share = (x_share.astype(jnp.float32) + attn_share).astype(jnp.bfloat16)
    resid = lax.all_to_all(
        jnp.broadcast_to(resid_share[:, None, :], (paired_rows, mp_count, column_share)),
        "mp",
        split_axis=1,
        concat_axis=1,
        tiled=True,
    ).reshape(paired_rows, features)
    resid_f = resid.astype(jnp.float32)
    stat = jnp.mean(resid_f * resid_f, axis=-1, keepdims=True)
    normed = (resid_f * lax.rsqrt(stat + 1e-06) * norm_gain).astype(jnp.bfloat16)
    logits = jnp.dot(normed, router, preferred_element_type=jnp.float32)
    expert_ids = routes.reshape(paired_rows, top_count)
    id_match = expert_ids[:, :, None] == lax.broadcasted_iota(jnp.int32, (1, 1, expert_total), 2)
    chosen = jnp.sum(jnp.where(id_match, logits[:, None, :], 0.0), axis=2)
    gates = jax.nn.softmax(chosen, axis=-1).astype(jnp.bfloat16)
    row_counts = jnp.sum(id_match.astype(jnp.int32), axis=1).reshape(steps, rows_dev, expert_total)
    before_count = (jnp.cumsum(row_counts, axis=1) - row_counts).reshape(
        paired_rows, 1, expert_total
    )
    rank_in_step = jnp.sum(jnp.where(id_match, before_count, 0), axis=2)
    step_index = lax.broadcasted_iota(jnp.int32, (steps, rows_dev, top_count), 0).reshape(
        paired_rows, top_count
    )
    target_slot = expert_ids * capacity + step_index * per_step_slots + rank_in_step
    slot_match = target_slot[:, :, None] == lax.broadcasted_iota(jnp.int32, (1, 1, slot_total), 2)
    spread_rows = jnp.any(slot_match, axis=1).astype(jnp.bfloat16)
    weigh_slots = jnp.sum(
        jnp.where(slot_match, gates[:, :, None].astype(jnp.float32), 0.0), axis=1
    ).astype(jnp.bfloat16)
    outgoing = jnp.einsum(
        "rabc,rf->abcf",
        spread_rows.reshape(paired_rows, expert_total, *slot_pack),
        normed,
        preferred_element_type=jnp.float32,
    ).astype(jnp.bfloat16)
    arrived = lax.all_to_all(outgoing, ("dy", "dx"), split_axis=0, concat_axis=0, tiled=True)
    gate_up = jnp.einsum(
        "abcf,fh->abch",
        arrived,
        relaid[:, :, : 2 * hid_group].reshape(features, 2 * hid_group),
        preferred_element_type=jnp.float32,
    )
    gate_out = gate_up[..., :hid_group]
    up_out = gate_up[..., hid_group:]
    hidden = (jax.nn.silu(gate_out) * up_out).astype(jnp.bfloat16).reshape(slot_total, hid_group)
    down_out = lax.dot_general(
        hidden, relaid[:, :, 2 * hid_group :].reshape(features, hid_group), (((1,), (1,)), ((), ())), preferred_element_type=jnp.float32
    )
    produced = down_out.astype(jnp.bfloat16).reshape(expert_total, *slot_pack, features)
    returned = lax.all_to_all(produced, ("dy", "dx"), split_axis=0, concat_axis=0, tiled=True)
    combined = jnp.einsum(
        "rabc,abcf->rf",
        weigh_slots.reshape(paired_rows, expert_total, *slot_pack),
        returned,
        preferred_element_type=jnp.float32,
    )
    shaped = combined.astype(jnp.bfloat16).reshape(paired_rows, mp_count, column_share)
    hidden_parts = lax.all_to_all(shaped, "mp", split_axis=1, concat_axis=1, tiled=True)
    moe_share = jnp.sum(hidden_parts.astype(jnp.float32), axis=1)
    mixed_out = (resid_share.astype(jnp.float32) + moe_share).astype(jnp.bfloat16)
    return mixed_out.reshape(steps, rows_dev, column_share)


def solution(mesh):
    inner = 8
    split_mesh = jax.sharding.Mesh(
        mesh.devices.reshape(mesh.shape["dp"] // inner, inner, mesh.shape["mp"]),
        ("dy", "dx", "mp"),
    )
    return jax.shard_map(
        shards,
        mesh=split_mesh,
        in_specs=(
            P(None, ("dy", "dx"), None),
            P(None, ("dy", "dx", "mp"), None, None),
            P(None, ("dy", "dx", "mp"), None, None),
            P(None, ("dy", "dx", "mp"), None, None),
            P(("dy", "dx", "mp"), None, None, None),
            P(("dy", "dx", "mp"), None, None, None),
            P(("dy", "dx", "mp")),
            P("mp", ("dy", "dx")),
            P(),
            P(),
            P(None, ("dy", "dx"), None),
            P(None, None, ("dy", "dx", "mp"), None),
        ),
        out_specs=P(None, ("dy", "dx"), "mp"),
        check_vma=False,
    )
```
